768 devices in a mesh: rad: 32 (over x_lo, y, core), az: 24 (over x_hi, z).
Axes of the slice: x: 4 (x_hi: 2, x_lo: 2; x = x_hi * 2 + x_lo), y: 8, z: 12, core: 2. Of those that a mesh axis runs over, the one named last changes fastest.
Arguments:
- fields: float32 [5, 192, 8, 6144], P(None, 'rad', None, 'az'), may hold values from -0.9 to 4, as said below
- shifts: int32 [192], P('rad'), may hold values from 0 to 768, as said below
Outputs:
- advanced: float32 [5, 192, 8, 6144], P(None, 'rad', None, 'az')
The draws below stay inside these ranges and needn't reach their ends.
Inputs may be any that keep to these rules, and one draw needn't show every extreme that they name: `fields`: components 0 (density) and 4 (pressure) lie in 2.0 to 4.0; components 1 to 3 (velocities) lie in -0.9 to 0.9. The first radius row shifts by 768 cells and the last one by 0.
All inputs are finite; a program needn't handle non-finite values.
Results may differ from the reference program's by a relative error of at most 0.0003.
Values sent between devices are 32-bit elements; how exact they have to be, the bound alone decides.
No kernel may reach another device: no remote copies, remote signals or barrier semaphores. Data moves between devices by JAX's collectives and lax.ppermute only.
A program may use at most 64 MiB of HBM per device.

```python
import math
import jax
import jax.numpy as jnp
from jax import lax

CR = 6
CTH = 8
CPHI = 256
STEPS = 1
NR = 192
NPHI = 6144
N_RAD = 32


def wave_field(key, periods, amplitude):
    phases = jax.random.uniform(key, (len(periods),), jnp.float32, 0.0, 2.0 * math.pi)
    radius = jnp.arange(NR, dtype=jnp.int32)[:, None, None]
    polar_index = jnp.arange(CTH, dtype=jnp.int32)[None, :, None]
    azimuth = jnp.arange(NPHI, dtype=jnp.int32)[None, None, :]
    layers = []
    for component in range(len(periods)):
        radial_period, polar_period, azimuth_period = periods[component]
        turning = (radius % radial_period).astype(jnp.float32) / radial_period
        turning = turning + (polar_index % polar_period).astype(jnp.float32) / polar_period
        turning = turning + (azimuth % azimuth_period).astype(jnp.float32) / azimuth_period
        layers.append(amplitude[component] * jnp.sin(2.0 * math.pi * turning + phases[component]))
    return jnp.stack(layers)


def draw_fields(key, part):
    split_keys = jax.random.split(jax.random.fold_in(key, 11), 2)
    grid_shape = (5, NR, CTH, NPHI)
    centre_values = jnp.array([3.0, 0.0, 0.0, 0.0, 3.0], dtype=jnp.float32)[:, None, None, None]
    smooth = wave_field(split_keys[1], [(10, 8, 12), (14, 6, 16), (9, 7, 11), (12, 5, 13), (11, 9, 10)], [0.55, 0.5, 0.5, 0.5, 0.55])
    rough = jnp.clip(0.15 * jax.random.normal(split_keys[0], grid_shape, jnp.float32), -0.4, 0.4)
    return (centre_values + smooth + rough).astype(jnp.float32)


def draw_shifts(key, part):
    row_index = jnp.arange(NR, dtype=jnp.int32)
    profile = 3 * CPHI * NR // (NR + 3 * row_index)
    jitter = jax.random.randint(jax.random.fold_in(key, 23), (NR,), 0, CPHI // 2 + 1)
    counts = jnp.clip(profile - jitter, 0, 3 * CPHI)
    counts = jnp.where(row_index == 0, 3 * CPHI, counts)
    return jnp.where(row_index == NR - 1, 0, counts).astype(jnp.int32)


def setup_inputs(seed: int = 0) -> dict:
    seeds = jax.random.split(jax.random.key(seed), 3)
    fields = draw_fields(jax.random.fold_in(seeds[2], 71), 0)
    shifts = draw_shifts(jax.random.fold_in(seeds[2], 71), 0)
    return dict(fields=fields, shifts=shifts)


ADIABATIC = 1.4
COURANT_RADIAL = 0.09
COURANT_POLAR = 0.08
COURANT_AZIMUTH = 0.18

def cut_along(values, first_cell, finish, along):
    return lax.slice_in_dim(values, first_cell, finish, axis=along)

def edge_states(values, along):
    length = values.shape[along]
    before = cut_along(values, 0, length - 3, along)
    centre = cut_along(values, 1, length - 2, along)
    follow = cut_along(values, 2, length - 1, along)
    beyond = cut_along(values, 3, length, along)
    interface = 7.0 / 12.0 * (centre + follow) - 1.0 / 12.0 * (before + beyond)
    interface = jnp.clip(interface, jnp.minimum(centre, follow), jnp.maximum(centre, follow))
    count = length - 3
    left_edge = cut_along(interface, 0, count - 1, along)
    right_edge = cut_along(interface, 1, count, along)
    middle_cell = cut_along(values, 2, length - 2, along)
    no_slope = (right_edge - middle_cell) * (middle_cell - left_edge) <= 0.0
    left_edge = jnp.where(no_slope, middle_cell, left_edge)
    right_edge = jnp.where(no_slope, middle_cell, right_edge)
    spread = right_edge - left_edge
    middle = middle_cell - 0.5 * (left_edge + right_edge)
    new_left = jnp.where(spread * middle > spread * spread / 6.0, 3.0 * middle_cell - 2.0 * right_edge, left_edge)
    new_right = jnp.where(spread * middle < -spread * spread / 6.0, 3.0 * middle_cell - 2.0 * left_edge, right_edge)
    return (new_left, new_right)

def primitive_parts(state, normal):
    density = state[0]
    pressure = state[4]
    normal_speed = state[normal]
    squared = state[1] * state[1] + state[2] * state[2] + state[3] * state[3]
    energy = pressure / (ADIABATIC - 1.0) + 0.5 * density * squared
    sound_speed = jnp.sqrt(ADIABATIC * pressure / density)
    conserved = [density, density * state[1], density * state[2], density * state[3], energy]
    flux_list = [plain_term * normal_speed for plain_term in conserved]
    flux_list[normal] = flux_list[normal] + pressure
    flux_list[4] = flux_list[4] + pressure * normal_speed
    return (density, pressure, normal_speed, energy, sound_speed, conserved, flux_list)

def star_flux(state, parts, wave_speed, contact, normal):
    density, pressure, normal_speed, energy, sound_speed, conserved, flux_list = parts
    factor = density * (wave_speed - normal_speed) / (wave_speed - contact)
    star_energy = factor * (energy / density + (contact - normal_speed) * (contact + pressure / (density * (wave_speed - normal_speed))))
    star_state = [factor, factor * state[1], factor * state[2], factor * state[3], star_energy]
    star_state[normal] = factor * contact
    return [flux_term + wave_speed * (star_term - plain_term) for flux_term, star_term, plain_term in zip(flux_list, star_state, conserved)]

def riemann_flux(left_state, right_state, normal):
    left_parts = primitive_parts(left_state, normal)
    right_parts = primitive_parts(right_state, normal)
    slow_wave = jnp.minimum(left_parts[2] - left_parts[4], right_parts[2] - right_parts[4])
    fast_wave = jnp.maximum(left_parts[2] + left_parts[4], right_parts[2] + right_parts[4])
    mass_left = left_parts[0] * (left_parts[2] - slow_wave)
    mass_right = right_parts[0] * (fast_wave - right_parts[2])
    contact = (mass_left * left_parts[2] + mass_right * right_parts[2] + left_parts[1] - right_parts[1]) / (mass_left + mass_right)
    star_left = star_flux(left_state, left_parts, slow_wave, contact, normal)
    star_right = star_flux(right_state, right_parts, fast_wave, contact, normal)
    merged = []
    for flux_left, inner_left, inner_right, flux_right in zip(left_parts[6], star_left, star_right, right_parts[6]):
        merged.append(jnp.where(slow_wave >= 0.0, flux_left, jnp.where(contact >= 0.0, inner_left, jnp.where(fast_wave > 0.0, inner_right, flux_right))))
    return jnp.stack(merged)

def flux_difference(window, along, normal):
    left_edge, right_edge = edge_states(window, along)
    cell_total = left_edge.shape[along]
    from_left = cut_along(right_edge, 0, cell_total - 1, along)
    from_right = cut_along(left_edge, 1, cell_total, along)
    flux_all = riemann_flux(from_left, from_right, normal)
    faces = flux_all.shape[along]
    return cut_along(flux_all, 1, faces, along) - cut_along(flux_all, 0, faces - 1, along)

def tendency(window, courant_rows):
    padded = jnp.pad(window, ((0, 0), (0, 0), (3, 3), (0, 0)), mode='edge')
    radial_term = flux_difference(padded[:, :, 3:-3, 3:-3], 1, 1)
    polar_term = flux_difference(padded[:, 3:-3, :, 3:-3], 2, 2)
    azimuth_term = flux_difference(padded[:, 3:-3, 3:-3, :], 3, 3)
    return -(COURANT_RADIAL * radial_term + COURANT_POLAR * polar_term + courant_rows[None, :, None, None] * azimuth_term)

def courant_profile(row_index, total_rows):
    return COURANT_AZIMUTH / (1.0 + (row_index + 0.5) / total_rows)

def to_conserved(primitive):
    density = primitive[0]
    squared = primitive[1] * primitive[1] + primitive[2] * primitive[2] + primitive[3] * primitive[3]
    energy = primitive[4] / (ADIABATIC - 1.0) + 0.5 * density * squared
    return jnp.stack([density, density * primitive[1], density * primitive[2], density * primitive[3], energy])

def to_primitive(conserved):
    density = conserved[0]
    velocity = conserved[1:4] / density
    squared = velocity[0] * velocity[0] + velocity[1] * velocity[1] + velocity[2] * velocity[2]
    pressure = (ADIABATIC - 1.0) * (conserved[4] - 0.5 * density * squared)
    return jnp.concatenate([density[None], velocity, pressure[None]])

def section_change(primitive, courant_all):
    padded = jnp.pad(primitive, ((0, 0), (3, 3), (0, 0), (0, 0)), mode='edge')
    padded = jnp.pad(padded, ((0, 0), (0, 0), (0, 0), (3, 3)), mode='wrap')

    def radial_block(block_index):
        window = lax.dynamic_slice_in_dim(padded, block_index * CR, CR + 6, axis=1)
        rows_here = lax.dynamic_slice_in_dim(courant_all, block_index * CR, CR)
        return tendency(window, rows_here)
    pieces = lax.map(radial_block, jnp.arange(N_RAD, dtype=jnp.int32))
    return jnp.moveaxis(pieces, 0, 1).reshape(primitive.shape)

def advect(primitive, shifts):

    def roll_row(one_row, amount):
        return jnp.roll(one_row, amount, axis=2)
    return jax.vmap(roll_row, in_axes=(1, 0), out_axes=1)(primitive, shifts)

def reference(fields, shifts):
    row_index = jnp.arange(NR, dtype=jnp.int32).astype(jnp.float32)
    courant_all = courant_profile(row_index, NR)
    current = fields
    for step_index in range(STEPS):
        initial = to_conserved(current)
        section_one = initial + section_change(current, courant_all)
        section_one_prim = to_primitive(section_one)
        section_two = 0.5 * initial + 0.5 * (section_one + section_change(section_one_prim, courant_all))
        current = advect(to_primitive(section_two), shifts)
    return current
```

```python
import jax
import jax.numpy as jnp
from jax import lax
from jax.sharding import PartitionSpec as P

ADIABATIC = 1.4
COURANT_RADIAL = 0.09
COURANT_POLAR = 0.08
COURANT_AZIMUTH = 0.18


def shifted(block, axis, distance):
    devices = range(lax.axis_size(axis))
    route = [((i - distance) % len(devices), i) for i in devices]
    return lax.ppermute(block, axis, route)


def cut_along(values, first_cell, finish, along):
    return lax.slice_in_dim(values, first_cell, finish, axis=along)


def edge_states(values, along):
    length = values.shape[along]
    before = cut_along(values, 0, length - 3, along)
    centre = cut_along(values, 1, length - 2, along)
    follow = cut_along(values, 2, length - 1, along)
    beyond = cut_along(values, 3, length, along)
    interface = 7.0 / 12.0 * (centre + follow) - 1.0 / 12.0 * (before + beyond)
    interface = jnp.clip(interface, jnp.minimum(centre, follow), jnp.maximum(centre, follow))
    count = length - 3
    left_edge = cut_along(interface, 0, count - 1, along)
    right_edge = cut_along(interface, 1, count, along)
    middle_cell = cut_along(values, 2, length - 2, along)
    no_slope = (right_edge - middle_cell) * (middle_cell - left_edge) <= 0.0
    left_edge = jnp.where(no_slope, middle_cell, left_edge)
    right_edge = jnp.where(no_slope, middle_cell, right_edge)
    spread = right_edge - left_edge
    middle = middle_cell - 0.5 * (left_edge + right_edge)
    new_left = jnp.where(
        spread * middle > spread * spread / 6.0, 3.0 * middle_cell - 2.0 * right_edge, left_edge
    )
    new_right = jnp.where(
        spread * middle < -spread * spread / 6.0, 3.0 * middle_cell - 2.0 * left_edge, right_edge
    )
    return (new_left, new_right)


def primitive_parts(state, normal):
    density = state[0]
    pressure = state[4]
    normal_speed = state[normal]
    squared = state[1] * state[1] + state[2] * state[2] + state[3] * state[3]
    energy = pressure / (ADIABATIC - 1.0) + 0.5 * density * squared
    sound_speed = jnp.sqrt(ADIABATIC * pressure / density)
    conserved = [density, density * state[1], density * state[2], density * state[3], energy]
    flux_list = [plain_term * normal_speed for plain_term in conserved]
    flux_list[normal] = flux_list[normal] + pressure
    flux_list[4] = flux_list[4] + pressure * normal_speed
    return (density, pressure, normal_speed, energy, sound_speed, conserved, flux_list)


def star_flux(state, parts, wave_speed, contact, normal):
    density, pressure, normal_speed, energy, sound_speed, conserved, flux_list = parts
    factor = density * (wave_speed - normal_speed) / (wave_speed - contact)
    star_energy = factor * (
        energy / density
        + (contact - normal_speed) * (contact + pressure / (density * (wave_speed - normal_speed)))
    )
    star_state = [factor, factor * state[1], factor * state[2], factor * state[3], star_energy]
    star_state[normal] = factor * contact
    return [
        flux_term + wave_speed * (star_term - plain_term)
        for flux_term, star_term, plain_term in zip(flux_list, star_state, conserved)
    ]


def riemann_flux(left_state, right_state, normal):
    left_parts = primitive_parts(left_state, normal)
    right_parts = primitive_parts(right_state, normal)
    slow_wave = jnp.minimum(left_parts[2] - left_parts[4], right_parts[2] - right_parts[4])
    fast_wave = jnp.maximum(left_parts[2] + left_parts[4], right_parts[2] + right_parts[4])
    mass_left = left_parts[0] * (left_parts[2] - slow_wave)
    mass_right = right_parts[0] * (fast_wave - right_parts[2])
    contact = (
        mass_left * left_parts[2] + mass_right * right_parts[2] + left_parts[1] - right_parts[1]
    ) / (mass_left + mass_right)
    star_left = star_flux(left_state, left_parts, slow_wave, contact, normal)
    star_right = star_flux(right_state, right_parts, fast_wave, contact, normal)
    merged = []
    for flux_left, inner_left, inner_right, flux_right in zip(
        left_parts[6], star_left, star_right, right_parts[6]
    ):
        merged.append(
            jnp.where(
                slow_wave >= 0.0,
                flux_left,
                jnp.where(
                    contact >= 0.0, inner_left, jnp.where(fast_wave > 0.0, inner_right, flux_right)
                ),
            )
        )
    return jnp.stack(merged)


def flux_difference(window, along, normal):
    left_edge, right_edge = edge_states(window, along)
    cell_total = left_edge.shape[along]
    from_left = cut_along(right_edge, 0, cell_total - 1, along)
    from_right = cut_along(left_edge, 1, cell_total, along)
    flux_all = riemann_flux(from_left, from_right, normal)
    faces = flux_all.shape[along]
    return cut_along(flux_all, 1, faces, along) - cut_along(flux_all, 0, faces - 1, along)


def tendency(window, courant_rows):
    padded = jnp.pad(window, ((0, 0), (0, 0), (3, 3), (0, 0)), mode="edge")
    radial_term = flux_difference(padded[:, :, 3:-3, 3:-3], 1, 1)
    polar_term = flux_difference(padded[:, 3:-3, :, 3:-3], 2, 2)
    azimuth_term = flux_difference(padded[:, 3:-3, 3:-3, :], 3, 3)
    return -(
        COURANT_RADIAL * radial_term
        + COURANT_POLAR * polar_term
        + courant_rows[None, :, None, None] * azimuth_term
    )


def courant_profile(row_index, total_rows):
    return COURANT_AZIMUTH / (1.0 + (row_index + 0.5) / total_rows)


def to_conserved(primitive):
    density = primitive[0]
    squared = (
        primitive[1] * primitive[1] + primitive[2] * primitive[2] + primitive[3] * primitive[3]
    )
    energy = primitive[4] / (ADIABATIC - 1.0) + 0.5 * density * squared
    return jnp.stack(
        [density, density * primitive[1], density * primitive[2], density * primitive[3], energy]
    )


def to_primitive(conserved):
    density = conserved[0]
    velocity = conserved[1:4] / density
    squared = velocity[0] * velocity[0] + velocity[1] * velocity[1] + velocity[2] * velocity[2]
    pressure = (ADIABATIC - 1.0) * (conserved[4] - 0.5 * density * squared)
    return jnp.concatenate([density[None], velocity, pressure[None]])


MAX_SHIFT = 768
HALO = 6


def ring_pairs(count, step, wrap):
    if wrap:
        return [(i, (i + step) % count) for i in range(count)]
    return [(i, i + step) for i in range(count) if 0 <= i + step < count]


def diagonal_pairs(n_rad, n_az, rad_step, az_step):
    pairs = []
    for r in range(n_rad):
        if not 0 <= r + rad_step < n_rad:
            continue
        for a in range(n_az):
            pairs.append((r * n_az + a, (r + rad_step) * n_az + (a + az_step) % n_az))
    return pairs


def clamp_rows(block, depth):
    rad_index = lax.axis_index("rad")
    last_index = lax.axis_size("rad") - 1
    rows = block.shape[1]
    lower = jnp.where(
        rad_index == 0,
        jnp.broadcast_to(block[:, depth : depth + 1], block[:, :depth].shape),
        block[:, :depth],
    )
    upper = jnp.where(
        rad_index == last_index,
        jnp.broadcast_to(block[:, rows - depth - 1 : rows - depth], block[:, rows - depth :].shape),
        block[:, rows - depth :],
    )
    return jnp.concatenate([lower, block[:, depth : rows - depth], upper], axis=1)


def extend_wide(x, width):
    n_rad, n_az = lax.axis_size("rad"), lax.axis_size("az")
    top = x[:, -width:]
    bottom = x[:, :width]
    from_below = lax.ppermute(top, "rad", ring_pairs(n_rad, 1, False))
    from_above = lax.ppermute(bottom, "rad", ring_pairs(n_rad, -1, False))
    from_left = lax.ppermute(x[..., -width:], "az", ring_pairs(n_az, 1, True))
    from_right = lax.ppermute(x[..., :width], "az", ring_pairs(n_az, -1, True))
    both = ("rad", "az")
    low_left = lax.ppermute(top[..., -width:], both, diagonal_pairs(n_rad, n_az, 1, 1))
    low_right = lax.ppermute(top[..., :width], both, diagonal_pairs(n_rad, n_az, 1, -1))
    up_left = lax.ppermute(bottom[..., -width:], both, diagonal_pairs(n_rad, n_az, -1, 1))
    up_right = lax.ppermute(bottom[..., :width], both, diagonal_pairs(n_rad, n_az, -1, -1))
    lower = jnp.concatenate([low_left, from_below, low_right], axis=3)
    middle = jnp.concatenate([from_left, x, from_right], axis=3)
    upper = jnp.concatenate([up_left, from_above, up_right], axis=3)
    return clamp_rows(jnp.concatenate([lower, middle, upper], axis=1), width)


def shift_rows(primitive, shifts):
    cell_count = primitive.shape[3]
    far = -(-MAX_SHIFT // cell_count)
    blocks = [primitive]
    for distance in range(1, far + 1):
        blocks.append(shifted(primitive, "az", distance))
    joined = jnp.concatenate(blocks[::-1], axis=3)
    width = joined.shape[3]
    source = lax.broadcasted_iota(jnp.int32, (1, width, cell_count), 1)
    target = lax.broadcasted_iota(jnp.int32, (1, width, cell_count), 2)
    start = far * cell_count - shifts
    pick = (source == target + start[:, None, None]).astype(jnp.float32)
    return jnp.einsum(
        "fitk,ikc->fitc",
        joined,
        pick,
        precision=lax.Precision.HIGHEST,
        preferred_element_type=jnp.float32,
    )


def on_device(fields, shifts):
    row_count = fields.shape[1]
    cell_count = fields.shape[3]
    rad_index = lax.axis_index("rad")
    total_rows = row_count * lax.axis_size("rad")
    half = HALO // 2
    wide_rows = (
        rad_index * row_count - half + jnp.arange(row_count + HALO, dtype=jnp.int32)
    ).astype(jnp.float32)
    courant_wide = courant_profile(wide_rows, total_rows)
    courant_inner = courant_wide[half : half + row_count]
    wide = extend_wide(fields, HALO)
    initial_wide = to_conserved(wide[:, half:-half, :, half:-half])
    section_one = initial_wide + tendency(wide, courant_wide)
    section_one_prim = clamp_rows(to_primitive(section_one), half)
    initial = initial_wide[:, half:-half, :, half:-half]
    section_one_inner = section_one[:, half:-half, :, half:-half]
    section_two = 0.5 * initial + 0.5 * (
        section_one_inner + tendency(section_one_prim, courant_inner)
    )
    return shift_rows(to_primitive(section_two), shifts)


def solution(mesh):
    in_specs = (P(None, "rad", None, "az"), P("rad"))
    out_specs = P(None, "rad", None, "az")
    return jax.shard_map(
        on_device, mesh=mesh, in_specs=in_specs, out_specs=out_specs, check_vma=False
    )
```

```python
import jax
import jax.numpy as jnp
from jax import lax
from jax.sharding import PartitionSpec as P

ADIABATIC = 1.4
COURANT_RADIAL = 0.09
COURANT_POLAR = 0.08
COURANT_AZIMUTH = 0.18


def shifted(block, axis, distance):
    devices = range(lax.axis_size(axis))
    route = [((i - distance) % len(devices), i) for i in devices]
    return lax.ppermute(block, axis, route)


def cut_along(values, first_cell, finish, along):
    return lax.slice_in_dim(values, first_cell, finish, axis=along)


def edge_states(values, along):
    length = values.shape[along]
    before = cut_along(values, 0, length - 3, along)
    centre = cut_along(values, 1, length - 2, along)
    follow = cut_along(values, 2, length - 1, along)
    beyond = cut_along(values, 3, length, along)
    interface = 7.0 / 12.0 * (centre + follow) - 1.0 / 12.0 * (before + beyond)
    interface = jnp.clip(interface, jnp.minimum(centre, follow), jnp.maximum(centre, follow))
    count = length - 3
    left_edge = cut_along(interface, 0, count - 1, along)
    right_edge = cut_along(interface, 1, count, along)
    middle_cell = cut_along(values, 2, length - 2, along)
    no_slope = (right_edge - middle_cell) * (middle_cell - left_edge) <= 0.0
    left_edge = jnp.where(no_slope, middle_cell, left_edge)
    right_edge = jnp.where(no_slope, middle_cell, right_edge)
    spread = right_edge - left_edge
    middle = middle_cell - 0.5 * (left_edge + right_edge)
    new_left = jnp.where(
        spread * middle > spread * spread / 6.0, 3.0 * middle_cell - 2.0 * right_edge, left_edge
    )
    new_right = jnp.where(
        spread * middle < -spread * spread / 6.0, 3.0 * middle_cell - 2.0 * left_edge, right_edge
    )
    return (new_left, new_right)


def primitive_parts(state, normal):
    density = state[0]
    pressure = state[4]
    normal_speed = state[normal]
    squared = state[1] * state[1] + state[2] * state[2] + state[3] * state[3]
    energy = pressure / (ADIABATIC - 1.0) + 0.5 * density * squared
    sound_speed = jnp.sqrt(ADIABATIC * pressure / density)
    conserved = [density, density * state[1], density * state[2], density * state[3], energy]
    flux_list = [plain_term * normal_speed for plain_term in conserved]
    flux_list[normal] = flux_list[normal] + pressure
    flux_list[4] = flux_list[4] + pressure * normal_speed
    return (density, pressure, normal_speed, energy, sound_speed, conserved, flux_list)


def star_flux(state, parts, wave_speed, contact, normal):
    density, pressure, normal_speed, energy, sound_speed, conserved, flux_list = parts
    factor = density * (wave_speed - normal_speed) / (wave_speed - contact)
    star_energy = factor * (
        energy / density
        + (contact - normal_speed) * (contact + pressure / (density * (wave_speed - normal_speed)))
    )
    star_state = [factor, factor * state[1], factor * state[2], factor * state[3], star_energy]
    star_state[normal] = factor * contact
    return [
        flux_term + wave_speed * (star_term - plain_term)
        for flux_term, star_term, plain_term in zip(flux_list, star_state, conserved)
    ]


def riemann_flux(left_state, right_state, normal):
    left_parts = primitive_parts(left_state, normal)
    right_parts = primitive_parts(right_state, normal)
    slow_wave = jnp.minimum(left_parts[2] - left_parts[4], right_parts[2] - right_parts[4])
    fast_wave = jnp.maximum(left_parts[2] + left_parts[4], right_parts[2] + right_parts[4])
    mass_left = left_parts[0] * (left_parts[2] - slow_wave)
    mass_right = right_parts[0] * (fast_wave - right_parts[2])
    contact = (
        mass_left * left_parts[2] + mass_right * right_parts[2] + left_parts[1] - right_parts[1]
    ) / (mass_left + mass_right)
    star_left = star_flux(left_state, left_parts, slow_wave, contact, normal)
    star_right = star_flux(right_state, right_parts, fast_wave, contact, normal)
    merged = []
    for flux_left, inner_left, inner_right, flux_right in zip(
        left_parts[6], star_left, star_right, right_parts[6]
    ):
        merged.append(
            jnp.where(
                slow_wave >= 0.0,
                flux_left,
                jnp.where(
                    contact >= 0.0, inner_left, jnp.where(fast_wave > 0.0, inner_right, flux_right)
                ),
            )
        )
    return jnp.stack(merged)


def flux_difference(window, along, normal):
    left_edge, right_edge = edge_states(window, along)
    cell_total = left_edge.shape[along]
    from_left = cut_along(right_edge, 0, cell_total - 1, along)
    from_right = cut_along(left_edge, 1, cell_total, along)
    flux_all = riemann_flux(from_left, from_right, normal)
    faces = flux_all.shape[along]
    return cut_along(flux_all, 1, faces, along) - cut_along(flux_all, 0, faces - 1, along)


def tendency(along_rad, along_az, inner, courant_rows):
    radial_term = flux_difference(along_rad, 1, 1)
    polar_term = flux_difference(jnp.pad(inner, ((0, 0), (0, 0), (3, 3), (0, 0)), mode="edge"), 2, 2)
    azimuth_term = flux_difference(along_az, 3, 3)
    return -(
        COURANT_RADIAL * radial_term
        + COURANT_POLAR * polar_term
        + courant_rows[None, :, None, None] * azimuth_term
    )


def courant_profile(row_index, total_rows):
    return COURANT_AZIMUTH / (1.0 + (row_index + 0.5) / total_rows)


def to_conserved(primitive):
    density = primitive[0]
    squared = (
        primitive[1] * primitive[1] + primitive[2] * primitive[2] + primitive[3] * primitive[3]
    )
    energy = primitive[4] / (ADIABATIC - 1.0) + 0.5 * density * squared
    return jnp.stack(
        [density, density * primitive[1], density * primitive[2], density * primitive[3], energy]
    )


def to_primitive(conserved):
    density = conserved[0]
    velocity = conserved[1:4] / density
    squared = velocity[0] * velocity[0] + velocity[1] * velocity[1] + velocity[2] * velocity[2]
    pressure = (ADIABATIC - 1.0) * (conserved[4] - 0.5 * density * squared)
    return jnp.concatenate([density[None], velocity, pressure[None]])


MAX_SHIFT = 768
HALO = 3


def ring_pairs(count, step, wrap):
    if wrap:
        return [(i, (i + step) % count) for i in range(count)]
    return [(i, i + step) for i in range(count) if 0 <= i + step < count]


def clamp_rows(block, depth):
    rad_index = lax.axis_index("rad")
    last_index = lax.axis_size("rad") - 1
    rows = block.shape[1]
    lower = jnp.where(
        rad_index == 0,
        jnp.broadcast_to(block[:, depth : depth + 1], block[:, :depth].shape),
        block[:, :depth],
    )
    upper = jnp.where(
        rad_index == last_index,
        jnp.broadcast_to(block[:, rows - depth - 1 : rows - depth], block[:, rows - depth :].shape),
        block[:, rows - depth :],
    )
    return jnp.concatenate([lower, block[:, depth : rows - depth], upper], axis=1)


def halos(x, width):
    n_rad, n_az = lax.axis_size("rad"), lax.axis_size("az")
    from_below = lax.ppermute(x[:, -width:], "rad", ring_pairs(n_rad, 1, False))
    from_above = lax.ppermute(x[:, :width], "rad", ring_pairs(n_rad, -1, False))
    from_left = lax.ppermute(x[..., -width:], "az", ring_pairs(n_az, 1, True))
    from_right = lax.ppermute(x[..., :width], "az", ring_pairs(n_az, -1, True))
    along_rad = clamp_rows(jnp.concatenate([from_below, x, from_above], axis=1), width)
    along_az = jnp.concatenate([from_left, x, from_right], axis=3)
    return along_rad, along_az


def change(x, courant_rows):
    along_rad, along_az = halos(x, HALO)
    return tendency(along_rad, along_az, x, courant_rows)


def shift_rows(primitive, shifts):
    cell_count = primitive.shape[3]
    far = -(-MAX_SHIFT // cell_count)
    blocks = [primitive]
    for distance in range(1, far + 1):
        if distance <= 2:
            blocks.append(shifted(primitive, "az", distance))
        else:
            blocks.append(shifted(blocks[-1], "az", 1))
    joined = jnp.concatenate(blocks[::-1], axis=3)
    width = joined.shape[3]
    source = lax.broadcasted_iota(jnp.int32, (1, width, cell_count), 1)
    target = lax.broadcasted_iota(jnp.int32, (1, width, cell_count), 2)
    start = far * cell_count - shifts
    pick = (source == target + start[:, None, None]).astype(jnp.float32)
    return jnp.einsum(
        "fitk,ikc->fitc",
        joined,
        pick,
        precision=lax.Precision.HIGHEST,
        preferred_element_type=jnp.float32,
    )


def on_device(fields, shifts):
    row_count = fields.shape[1]
    rad_index = lax.axis_index("rad")
    total_rows = row_count * lax.axis_size("rad")
    inner_rows = (rad_index * row_count + jnp.arange(row_count, dtype=jnp.int32)).astype(
        jnp.float32
    )
    courant_inner = courant_profile(inner_rows, total_rows)
    initial = to_conserved(fields)
    section_one = initial + change(fields, courant_inner)
    section_one_prim = to_primitive(section_one)
    section_two = 0.5 * initial + 0.5 * (section_one + change(section_one_prim, courant_inner))
    return shift_rows(to_primitive(section_two), shifts)


def solution(mesh):
    in_specs = (P(None, "rad", None, "az"), P("rad"))
    out_specs = P(None, "rad", None, "az")
    return jax.shard_map(
        on_device, mesh=mesh, in_specs=in_specs, out_specs=out_specs, check_vma=False
    )
```

```python
import jax
import jax.numpy as jnp
from jax import lax
from jax.sharding import PartitionSpec as P

ADIABATIC = 1.4
COURANT_RADIAL = 0.09
COURANT_POLAR = 0.08
COURANT_AZIMUTH = 0.18


def shifted(block, axis, distance):
    devices = range(lax.axis_size(axis))
    route = [((i - distance) % len(devices), i) for i in devices]
    return lax.ppermute(block, axis, route)


def cut_along(values, first_cell, finish, along):
    return lax.slice_in_dim(values, first_cell, finish, axis=along)


def edge_states(values, along):
    length = values.shape[along]
    before = cut_along(values, 0, length - 3, along)
    centre = cut_along(values, 1, length - 2, along)
    follow = cut_along(values, 2, length - 1, along)
    beyond = cut_along(values, 3, length, along)
    interface = 7.0 / 12.0 * (centre + follow) - 1.0 / 12.0 * (before + beyond)
    interface = jnp.clip(interface, jnp.minimum(centre, follow), jnp.maximum(centre, follow))
    count = length - 3
    left_edge = cut_along(interface, 0, count - 1, along)
    right_edge = cut_along(interface, 1, count, along)
    middle_cell = cut_along(values, 2, length - 2, along)
    no_slope = (right_edge - middle_cell) * (middle_cell - left_edge) <= 0.0
    left_edge = jnp.where(no_slope, middle_cell, left_edge)
    right_edge = jnp.where(no_slope, middle_cell, right_edge)
    spread = right_edge - left_edge
    middle = middle_cell - 0.5 * (left_edge + right_edge)
    new_left = jnp.where(
        spread * middle > spread * spread / 6.0, 3.0 * middle_cell - 2.0 * right_edge, left_edge
    )
    new_right = jnp.where(
        spread * middle < -spread * spread / 6.0, 3.0 * middle_cell - 2.0 * left_edge, right_edge
    )
    return (new_left, new_right)


def primitive_parts(state, normal):
    density = state[0]
    pressure = state[4]
    normal_speed = state[normal]
    squared = state[1] * state[1] + state[2] * state[2] + state[3] * state[3]
    energy = pressure / (ADIABATIC - 1.0) + 0.5 * density * squared
    sound_speed = jnp.sqrt(ADIABATIC * pressure / density)
    conserved = [density, density * state[1], density * state[2], density * state[3], energy]
    flux_list = [plain_term * normal_speed for plain_term in conserved]
    flux_list[normal] = flux_list[normal] + pressure
    flux_list[4] = flux_list[4] + pressure * normal_speed
    return (density, pressure, normal_speed, energy, sound_speed, conserved, flux_list)


def star_flux(state, parts, wave_speed, contact, normal):
    density, pressure, normal_speed, energy, sound_speed, conserved, flux_list = parts
    factor = density * (wave_speed - normal_speed) / (wave_speed - contact)
    star_energy = factor * (
        energy / density
        + (contact - normal_speed) * (contact + pressure / (density * (wave_speed - normal_speed)))
    )
    star_state = [factor, factor * state[1], factor * state[2], factor * state[3], star_energy]
    star_state[normal] = factor * contact
    return [
        flux_term + wave_speed * (star_term - plain_term)
        for flux_term, star_term, plain_term in zip(flux_list, star_state, conserved)
    ]


def riemann_flux(left_state, right_state, normal):
    left_parts = primitive_parts(left_state, normal)
    right_parts = primitive_parts(right_state, normal)
    slow_wave = jnp.minimum(left_parts[2] - left_parts[4], right_parts[2] - right_parts[4])
    fast_wave = jnp.maximum(left_parts[2] + left_parts[4], right_parts[2] + right_parts[4])
    mass_left = left_parts[0] * (left_parts[2] - slow_wave)
    mass_right = right_parts[0] * (fast_wave - right_parts[2])
    contact = (
        mass_left * left_parts[2] + mass_right * right_parts[2] + left_parts[1] - right_parts[1]
    ) / (mass_left + mass_right)
    star_left = star_flux(left_state, left_parts, slow_wave, contact, normal)
    star_right = star_flux(right_state, right_parts, fast_wave, contact, normal)
    merged = []
    for flux_left, inner_left, inner_right, flux_right in zip(
        left_parts[6], star_left, star_right, right_parts[6]
    ):
        merged.append(
            jnp.where(
                slow_wave >= 0.0,
                flux_left,
                jnp.where(
                    contact >= 0.0, inner_left, jnp.where(fast_wave > 0.0, inner_right, flux_right)
                ),
            )
        )
    return jnp.stack(merged)


def flux_difference(window, along, normal):
    left_edge, right_edge = edge_states(window, along)
    cell_total = left_edge.shape[along]
    from_left = cut_along(right_edge, 0, cell_total - 1, along)
    from_right = cut_along(left_edge, 1, cell_total, along)
    flux_all = riemann_flux(from_left, from_right, normal)
    faces = flux_all.shape[along]
    return cut_along(flux_all, 1, faces, along) - cut_along(flux_all, 0, faces - 1, along)


def tendency(along_rad, along_az, inner, courant_rows):
    radial_term = flux_difference(along_rad, 1, 1)
    polar_term = flux_difference(jnp.pad(inner, ((0, 0), (0, 0), (3, 3), (0, 0)), mode="edge"), 2, 2)
    azimuth_term = flux_difference(along_az, 3, 3)
    return -(
        COURANT_RADIAL * radial_term
        + COURANT_POLAR * polar_term
        + courant_rows[None, :, None, None] * azimuth_term
    )


def courant_profile(row_index, total_rows):
    return COURANT_AZIMUTH / (1.0 + (row_index + 0.5) / total_rows)


def to_conserved(primitive):
    density = primitive[0]
    squared = (
        primitive[1] * primitive[1] + primitive[2] * primitive[2] + primitive[3] * primitive[3]
    )
    energy = primitive[4] / (ADIABATIC - 1.0) + 0.5 * density * squared
    return jnp.stack(
        [density, density * primitive[1], density * primitive[2], density * primitive[3], energy]
    )


def to_primitive(conserved):
    density = conserved[0]
    velocity = conserved[1:4] / density
    squared = velocity[0] * velocity[0] + velocity[1] * velocity[1] + velocity[2] * velocity[2]
    pressure = (ADIABATIC - 1.0) * (conserved[4] - 0.5 * density * squared)
    return jnp.concatenate([density[None], velocity, pressure[None]])


MAX_SHIFT = 768
HALO = 3


def ring_pairs(count, step, wrap):
    if wrap:
        return [(i, (i + step) % count) for i in range(count)]
    return [(i, i + step) for i in range(count) if 0 <= i + step < count]


def clamp_rows(block, depth):
    rad_index = lax.axis_index("rad")
    last_index = lax.axis_size("rad") - 1
    rows = block.shape[1]
    lower = jnp.where(
        rad_index == 0,
        jnp.broadcast_to(block[:, depth : depth + 1], block[:, :depth].shape),
        block[:, :depth],
    )
    upper = jnp.where(
        rad_index == last_index,
        jnp.broadcast_to(block[:, rows - depth - 1 : rows - depth], block[:, rows - depth :].shape),
        block[:, rows - depth :],
    )
    return jnp.concatenate([lower, block[:, depth : rows - depth], upper], axis=1)


def halos(x, width):
    n_rad, n_az = lax.axis_size("rad"), lax.axis_size("az")
    from_below = lax.ppermute(x[:, -width:], "rad", ring_pairs(n_rad, 1, False))
    from_above = lax.ppermute(x[:, :width], "rad", ring_pairs(n_rad, -1, False))
    from_left = lax.ppermute(x[..., -width:], "az", ring_pairs(n_az, 1, True))
    from_right = lax.ppermute(x[..., :width], "az", ring_pairs(n_az, -1, True))
    along_rad = clamp_rows(jnp.concatenate([from_below, x, from_above], axis=1), width)
    along_az = jnp.concatenate([from_left, x, from_right], axis=3)
    return along_rad, along_az


def change(x, courant_rows):
    along_rad, along_az = halos(x, HALO)
    return tendency(along_rad, along_az, x, courant_rows)


def shift_rows(primitive, shifts):
    cell_count = primitive.shape[3]
    far = -(-MAX_SHIFT // cell_count)
    blocks = [primitive]
    for distance in range(1, far + 1):
        if distance <= 2:
            blocks.append(shifted(primitive, "az", distance))
        else:
            blocks.append(shifted(blocks[-1], "az", 1))
    joined = jnp.concatenate(blocks[::-1], axis=3)
    width = joined.shape[3]
    source = lax.broadcasted_iota(jnp.int32, (1, width, cell_count), 1)
    target = lax.broadcasted_iota(jnp.int32, (1, width, cell_count), 2)
    start = far * cell_count - shifts
    pick = (source == target + start[:, None, None]).astype(jnp.float32)
    return jnp.einsum(
        "fitk,ikc->fitc",
        joined,
        pick,
        precision=lax.Precision.HIGHEST,
        preferred_element_type=jnp.float32,
    )


def extend_wide(x, width):
    n_rad, n_az = lax.axis_size("rad"), lax.axis_size("az")
    from_below = lax.ppermute(x[:, -width:], "rad", ring_pairs(n_rad, 1, False))
    from_above = lax.ppermute(x[:, :width], "rad", ring_pairs(n_rad, -1, False))
    rows = clamp_rows(jnp.concatenate([from_below, x, from_above], axis=1), width)
    from_left = lax.ppermute(rows[..., -width:], "az", ring_pairs(n_az, 1, True))
    from_right = lax.ppermute(rows[..., :width], "az", ring_pairs(n_az, -1, True))
    return jnp.concatenate([from_left, rows, from_right], axis=3)


def local_change(window, courant_rows):
    depth = HALO
    along_rad = window[..., depth:-depth]
    along_az = window[:, depth:-depth]
    inner = window[:, depth:-depth, :, depth:-depth]
    return tendency(along_rad, along_az, inner, courant_rows)


def on_device(fields, shifts):
    row_count = fields.shape[1]
    rad_index = lax.axis_index("rad")
    total_rows = row_count * lax.axis_size("rad")
    depth = HALO
    wide_rows = (
        rad_index * row_count - depth + jnp.arange(row_count + 2 * depth, dtype=jnp.int32)
    ).astype(jnp.float32)
    courant_wide = courant_profile(wide_rows, total_rows)
    courant_inner = courant_wide[depth : depth + row_count]
    wide = extend_wide(fields, 2 * depth)
    initial_wide = to_conserved(wide[:, depth:-depth, :, depth:-depth])
    section_one = initial_wide + local_change(wide, courant_wide)
    section_one_prim = clamp_rows(to_primitive(section_one), depth)
    initial = initial_wide[:, depth:-depth, :, depth:-depth]
    section_one_inner = section_one[:, depth:-depth, :, depth:-depth]
    section_two = 0.5 * initial + 0.5 * (
        section_one_inner + local_change(section_one_prim, courant_inner)
    )
    return shift_rows(to_primitive(section_two), shifts)


def solution(mesh):
    in_specs = (P(None, "rad", None, "az"), P("rad"))
    out_specs = P(None, "rad", None, "az")
    return jax.shard_map(
        on_device, mesh=mesh, in_specs=in_specs, out_specs=out_specs, check_vma=False
    )
```

```python
import jax
import jax.numpy as jnp
from jax import lax
from jax.sharding import PartitionSpec as P

ADIABATIC = 1.4
COURANT_RADIAL = 0.09
COURANT_POLAR = 0.08
COURANT_AZIMUTH = 0.18


def shifted(block, axis, distance):
    devices = range(lax.axis_size(axis))
    route = [((i - distance) % len(devices), i) for i in devices]
    return lax.ppermute(block, axis, route)


def cut_along(values, first_cell, finish, along):
    return lax.slice_in_dim(values, first_cell, finish, axis=along)


def edge_states(values, along):
    length = values.shape[along]
    before = cut_along(values, 0, length - 3, along)
    centre = cut_along(values, 1, length - 2, along)
    follow = cut_along(values, 2, length - 1, along)
    beyond = cut_along(values, 3, length, along)
    interface = 7.0 / 12.0 * (centre + follow) - 1.0 / 12.0 * (before + beyond)
    interface = jnp.clip(interface, jnp.minimum(centre, follow), jnp.maximum(centre, follow))
    count = length - 3
    left_edge = cut_along(interface, 0, count - 1, along)
    right_edge = cut_along(interface, 1, count, along)
    middle_cell = cut_along(values, 2, length - 2, along)
    no_slope = (right_edge - middle_cell) * (middle_cell - left_edge) <= 0.0
    left_edge = jnp.where(no_slope, middle_cell, left_edge)
    right_edge = jnp.where(no_slope, middle_cell, right_edge)
    spread = right_edge - left_edge
    middle = middle_cell - 0.5 * (left_edge + right_edge)
    new_left = jnp.where(
        spread * middle > spread * spread / 6.0, 3.0 * middle_cell - 2.0 * right_edge, left_edge
    )
    new_right = jnp.where(
        spread * middle < -spread * spread / 6.0, 3.0 * middle_cell - 2.0 * left_edge, right_edge
    )
    return (new_left, new_right)


def primitive_parts(state, normal):
    density = state[0]
    pressure = state[4]
    normal_speed = state[normal]
    squared = state[1] * state[1] + state[2] * state[2] + state[3] * state[3]
    energy = pressure / (ADIABATIC - 1.0) + 0.5 * density * squared
    sound_speed = jnp.sqrt(ADIABATIC * pressure / density)
    conserved = [density, density * state[1], density * state[2], density * state[3], energy]
    flux_list = [plain_term * normal_speed for plain_term in conserved]
    flux_list[normal] = flux_list[normal] + pressure
    flux_list[4] = flux_list[4] + pressure * normal_speed
    return (density, pressure, normal_speed, energy, sound_speed, conserved, flux_list)


def star_flux(state, parts, wave_speed, contact, normal):
    density, pressure, normal_speed, energy, sound_speed, conserved, flux_list = parts
    factor = density * (wave_speed - normal_speed) / (wave_speed - contact)
    star_energy = factor * (
        energy / density
        + (contact - normal_speed) * (contact + pressure / (density * (wave_speed - normal_speed)))
    )
    star_state = [factor, factor * state[1], factor * state[2], factor * state[3], star_energy]
    star_state[normal] = factor * contact
    return [
        flux_term + wave_speed * (star_term - plain_term)
        for flux_term, star_term, plain_term in zip(flux_list, star_state, conserved)
    ]


def riemann_flux(left_state, right_state, normal):
    left_parts = primitive_parts(left_state, normal)
    right_parts = primitive_parts(right_state, normal)
    slow_wave = jnp.minimum(left_parts[2] - left_parts[4], right_parts[2] - right_parts[4])
    fast_wave = jnp.maximum(left_parts[2] + left_parts[4], right_parts[2] + right_parts[4])
    mass_left = left_parts[0] * (left_parts[2] - slow_wave)
    mass_right = right_parts[0] * (fast_wave - right_parts[2])
    contact = (
        mass_left * left_parts[2] + mass_right * right_parts[2] + left_parts[1] - right_parts[1]
    ) / (mass_left + mass_right)
    star_left = star_flux(left_state, left_parts, slow_wave, contact, normal)
    star_right = star_flux(right_state, right_parts, fast_wave, contact, normal)
    merged = []
    for flux_left, inner_left, inner_right, flux_right in zip(
        left_parts[6], star_left, star_right, right_parts[6]
    ):
        merged.append(
            jnp.where(
                slow_wave >= 0.0,
                flux_left,
                jnp.where(
                    contact >= 0.0, inner_left, jnp.where(fast_wave > 0.0, inner_right, flux_right)
                ),
            )
        )
    return jnp.stack(merged)


def flux_difference(window, along, normal):
    left_edge, right_edge = edge_states(window, along)
    cell_total = left_edge.shape[along]
    from_left = cut_along(right_edge, 0, cell_total - 1, along)
    from_right = cut_along(left_edge, 1, cell_total, along)
    flux_all = riemann_flux(from_left, from_right, normal)
    faces = flux_all.shape[along]
    return cut_along(flux_all, 1, faces, along) - cut_along(flux_all, 0, faces - 1, along)


def tendency(along_rad, along_az, inner, courant_rows):
    radial_term = flux_difference(along_rad, 1, 1)
    polar_term = flux_difference(jnp.pad(inner, ((0, 0), (0, 0), (3, 3), (0, 0)), mode="edge"), 2, 2)
    azimuth_term = flux_difference(along_az, 3, 3)
    return -(
        COURANT_RADIAL * radial_term
        + COURANT_POLAR * polar_term
        + courant_rows[None, :, None, None] * azimuth_term
    )


def courant_profile(row_index, total_rows):
    return COURANT_AZIMUTH / (1.0 + (row_index + 0.5) / total_rows)


def to_conserved(primitive):
    density = primitive[0]
    squared = (
        primitive[1] * primitive[1] + primitive[2] * primitive[2] + primitive[3] * primitive[3]
    )
    energy = primitive[4] / (ADIABATIC - 1.0) + 0.5 * density * squared
    return jnp.stack(
        [density, density * primitive[1], density * primitive[2], density * primitive[3], energy]
    )


def to_primitive(conserved):
    density = conserved[0]
    velocity = conserved[1:4] / density
    squared = velocity[0] * velocity[0] + velocity[1] * velocity[1] + velocity[2] * velocity[2]
    pressure = (ADIABATIC - 1.0) * (conserved[4] - 0.5 * density * squared)
    return jnp.concatenate([density[None], velocity, pressure[None]])


MAX_SHIFT = 768
HALO = 3


def ring_pairs(count, step, wrap):
    if wrap:
        return [(i, (i + step) % count) for i in range(count)]
    return [(i, i + step) for i in range(count) if 0 <= i + step < count]


def clamp_rows(block, depth):
    rad_index = lax.axis_index("rad")
    last_index = lax.axis_size("rad") - 1
    rows = block.shape[1]
    lower = jnp.where(
        rad_index == 0,
        jnp.broadcast_to(block[:, depth : depth + 1], block[:, :depth].shape),
        block[:, :depth],
    )
    upper = jnp.where(
        rad_index == last_index,
        jnp.broadcast_to(block[:, rows - depth - 1 : rows - depth], block[:, rows - depth :].shape),
        block[:, rows - depth :],
    )
    return jnp.concatenate([lower, block[:, depth : rows - depth], upper], axis=1)


def halos(x, width):
    n_rad, n_az = lax.axis_size("rad"), lax.axis_size("az")
    from_below = lax.ppermute(x[:, -width:], "rad", ring_pairs(n_rad, 1, False))
    from_above = lax.ppermute(x[:, :width], "rad", ring_pairs(n_rad, -1, False))
    from_left = lax.ppermute(x[..., -width:], "az", ring_pairs(n_az, 1, True))
    from_right = lax.ppermute(x[..., :width], "az", ring_pairs(n_az, -1, True))
    along_rad = clamp_rows(jnp.concatenate([from_below, x, from_above], axis=1), width)
    along_az = jnp.concatenate([from_left, x, from_right], axis=3)
    return along_rad, along_az


def change(x, courant_rows):
    along_rad, along_az = halos(x, HALO)
    return tendency(along_rad, along_az, x, courant_rows)


def shift_rows(primitive, shifts):
    cell_count = primitive.shape[3]
    far = -(-MAX_SHIFT // cell_count)
    blocks = [primitive]
    for distance in range(1, far + 1):
        if distance <= 2:
            blocks.append(shifted(primitive, "az", distance))
        else:
            blocks.append(shifted(blocks[-1], "az", 1))
    source = lax.broadcasted_iota(jnp.int32, (1, cell_count, cell_count), 1)
    target = lax.broadcasted_iota(jnp.int32, (1, cell_count, cell_count), 2)
    offset = source - target + shifts[:, None, None]
    total = None
    for distance, block in enumerate(blocks):
        pick = (offset == distance * cell_count).astype(jnp.float32)
        part = jnp.einsum(
            "fitk,ikc->fitc",
            block,
            pick,
            precision=lax.Precision.HIGHEST,
            preferred_element_type=jnp.float32,
        )
        total = part if total is None else total + part
    return total


def on_device(fields, shifts):
    row_count = fields.shape[1]
    rad_index = lax.axis_index("rad")
    total_rows = row_count * lax.axis_size("rad")
    inner_rows = (rad_index * row_count + jnp.arange(row_count, dtype=jnp.int32)).astype(
        jnp.float32
    )
    courant_inner = courant_profile(inner_rows, total_rows)
    initial = to_conserved(fields)
    section_one = initial + change(fields, courant_inner)
    section_one_prim = to_primitive(section_one)
    section_two = 0.5 * initial + 0.5 * (section_one + change(section_one_prim, courant_inner))
    return shift_rows(to_primitive(section_two), shifts)


def solution(mesh):
    in_specs = (P(None, "rad", None, "az"), P("rad"))
    out_specs = P(None, "rad", None, "az")
    return jax.shard_map(
        on_device, mesh=mesh, in_specs=in_specs, out_specs=out_specs, check_vma=False
    )
```

```python
import jax
import jax.numpy as jnp
from jax import lax
from jax.sharding import PartitionSpec as P


ADIABATIC = 1.4
COURANT_RADIAL = 0.09
COURANT_POLAR = 0.08
COURANT_AZIMUTH = 0.18


def shifted(block, axis, distance):
    devices = range(lax.axis_size(axis))
    route = [((i - distance) % len(devices), i) for i in devices]
    return lax.ppermute(block, axis, route)


def cut_along(values, first_cell, finish, along):
    return lax.slice_in_dim(values, first_cell, finish, axis=along)


def edge_states(values, along):
    length = values.shape[along]
    before = cut_along(values, 0, length - 3, along)
    centre = cut_along(values, 1, length - 2, along)
    follow = cut_along(values, 2, length - 1, along)
    beyond = cut_along(values, 3, length, along)
    interface = 7.0 / 12.0 * (centre + follow) - 1.0 / 12.0 * (before + beyond)
    interface = jnp.clip(interface, jnp.minimum(centre, follow), jnp.maximum(centre, follow))
    count = length - 3
    left_edge = cut_along(interface, 0, count - 1, along)
    right_edge = cut_along(interface, 1, count, along)
    middle_cell = cut_along(values, 2, length - 2, along)
    no_slope = (right_edge - middle_cell) * (middle_cell - left_edge) <= 0.0
    left_edge = jnp.where(no_slope, middle_cell, left_edge)
    right_edge = jnp.where(no_slope, middle_cell, right_edge)
    spread = right_edge - left_edge
    middle = middle_cell - 0.5 * (left_edge + right_edge)
    new_left = jnp.where(
        spread * middle > spread * spread / 6.0, 3.0 * middle_cell - 2.0 * right_edge, left_edge
    )
    new_right = jnp.where(
        spread * middle < -spread * spread / 6.0, 3.0 * middle_cell - 2.0 * left_edge, right_edge
    )
    return (new_left, new_right)


def primitive_parts(state, normal):
    density = state[0]
    pressure = state[4]
    normal_speed = state[normal]
    squared = state[1] * state[1] + state[2] * state[2] + state[3] * state[3]
    energy = pressure / (ADIABATIC - 1.0) + 0.5 * density * squared
    sound_speed = jnp.sqrt(ADIABATIC * pressure / density)
    conserved = [density, density * state[1], density * state[2], density * state[3], energy]
    flux_list = [plain_term * normal_speed for plain_term in conserved]
    flux_list[normal] = flux_list[normal] + pressure
    flux_list[4] = flux_list[4] + pressure * normal_speed
    return (density, pressure, normal_speed, energy, sound_speed, conserved, flux_list)


def star_flux(state, parts, wave_speed, contact, normal):
    density, pressure, normal_speed, energy, _, conserved, flux_list = parts
    factor = density * (wave_speed - normal_speed) / (wave_speed - contact)
    star_energy = factor * (
        energy / density
        + (contact - normal_speed) * (contact + pressure / (density * (wave_speed - normal_speed)))
    )
    star_state = [factor, factor * state[1], factor * state[2], factor * state[3], star_energy]
    star_state[normal] = factor * contact
    return [
        flux_term + wave_speed * (star_term - plain_term)
        for flux_term, star_term, plain_term in zip(flux_list, star_state, conserved)
    ]


def riemann_flux(left_state, right_state, normal):
    left_parts = primitive_parts(left_state, normal)
    right_parts = primitive_parts(right_state, normal)
    slow_wave = jnp.minimum(left_parts[2] - left_parts[4], right_parts[2] - right_parts[4])
    fast_wave = jnp.maximum(left_parts[2] + left_parts[4], right_parts[2] + right_parts[4])
    mass_left = left_parts[0] * (left_parts[2] - slow_wave)
    mass_right = right_parts[0] * (fast_wave - right_parts[2])
    contact = (
        mass_left * left_parts[2] + mass_right * right_parts[2] + left_parts[1] - right_parts[1]
    ) / (mass_left + mass_right)
    star_left = star_flux(left_state, left_parts, slow_wave, contact, normal)
    star_right = star_flux(right_state, right_parts, fast_wave, contact, normal)
    merged = []
    for flux_left, inner_left, inner_right, flux_right in zip(
        left_parts[6], star_left, star_right, right_parts[6]
    ):
        merged.append(
            jnp.where(
                slow_wave >= 0.0,
                flux_left,
                jnp.where(
                    contact >= 0.0, inner_left, jnp.where(fast_wave > 0.0, inner_right, flux_right)
                ),
            )
        )
    return jnp.stack(merged)


def flux_difference(window, along, normal):
    left_edge, right_edge = edge_states(window, along)
    cell_total = left_edge.shape[along]
    from_left = cut_along(right_edge, 0, cell_total - 1, along)
    from_right = cut_along(left_edge, 1, cell_total, along)
    flux_all = riemann_flux(from_left, from_right, normal)
    faces = flux_all.shape[along]
    return cut_along(flux_all, 1, faces, along) - cut_along(flux_all, 0, faces - 1, along)


def tendency(along_rad, along_az, inner, courant_rows):
    radial_term = flux_difference(along_rad, 1, 1)
    polar_term = flux_difference(jnp.pad(inner, ((0, 0), (0, 0), (3, 3), (0, 0)), mode="edge"), 2, 2)
    azimuth_term = flux_difference(along_az, 3, 3)
    return -(
        COURANT_RADIAL * radial_term
        + COURANT_POLAR * polar_term
        + courant_rows[None, :, None, None] * azimuth_term
    )


def courant_profile(row_index, total_rows):
    return COURANT_AZIMUTH / (1.0 + (row_index + 0.5) / total_rows)


def to_conserved(primitive):
    density = primitive[0]
    squared = (
        primitive[1] * primitive[1] + primitive[2] * primitive[2] + primitive[3] * primitive[3]
    )
    energy = primitive[4] / (ADIABATIC - 1.0) + 0.5 * density * squared
    return jnp.stack(
        [density, density * primitive[1], density * primitive[2], density * primitive[3], energy]
    )


def to_primitive(conserved):
    density = conserved[0]
    velocity = conserved[1:4] / density
    squared = velocity[0] * velocity[0] + velocity[1] * velocity[1] + velocity[2] * velocity[2]
    pressure = (ADIABATIC - 1.0) * (conserved[4] - 0.5 * density * squared)
    return jnp.concatenate([density[None], velocity, pressure[None]])


MAX_SHIFT = 768
HALO = 3


def ring_pairs(count, step, wrap):
    if wrap:
        return [(i, (i + step) % count) for i in range(count)]
    return [(i, i + step) for i in range(count) if 0 <= i + step < count]


def clamp_rows(block, depth):
    rad_index = lax.axis_index("rad")
    last_index = lax.axis_size("rad") - 1
    rows = block.shape[1]
    lower = jnp.where(
        rad_index == 0,
        jnp.broadcast_to(block[:, depth : depth + 1], block[:, :depth].shape),
        block[:, :depth],
    )
    upper = jnp.where(
        rad_index == last_index,
        jnp.broadcast_to(block[:, rows - depth - 1 : rows - depth], block[:, rows - depth :].shape),
        block[:, rows - depth :],
    )
    return jnp.concatenate([lower, block[:, depth : rows - depth], upper], axis=1)


def flat_ppermute(block, axis, pairs):
    return lax.ppermute(block.reshape(-1), axis, pairs).reshape(block.shape)


def halos(x, width):
    n_rad, n_az = lax.axis_size("rad"), lax.axis_size("az")
    from_below = lax.ppermute(x[:, -width:], "rad", ring_pairs(n_rad, 1, False))
    from_above = lax.ppermute(x[:, :width], "rad", ring_pairs(n_rad, -1, False))
    from_left = flat_ppermute(x[..., -width:], "az", ring_pairs(n_az, 1, True))
    from_right = flat_ppermute(x[..., :width], "az", ring_pairs(n_az, -1, True))
    along_rad = clamp_rows(jnp.concatenate([from_below, x, from_above], axis=1), width)
    along_az = jnp.concatenate([from_left, x, from_right], axis=3)
    return along_rad, along_az


def change(x, courant_rows):
    along_rad, along_az = halos(x, HALO)
    return tendency(along_rad, along_az, x, courant_rows)


def shift_rows(primitive, shifts):
    cell_count = primitive.shape[3]
    far = -(-MAX_SHIFT // cell_count)
    blocks = [primitive]
    for distance in range(1, far + 1):
        if distance <= 2:
            blocks.append(shifted(primitive, "az", distance))
        else:
            blocks.append(shifted(blocks[-1], "az", 1))
    source = lax.broadcasted_iota(jnp.int32, (1, cell_count, cell_count), 1)
    target = lax.broadcasted_iota(jnp.int32, (1, cell_count, cell_count), 2)
    offset = source - target + shifts[:, None, None]
    total = None
    for distance, block in enumerate(blocks):
        pick = (offset == distance * cell_count).astype(jnp.float32)
        part = jnp.einsum(
            "fitk,ikc->fitc",
            block,
            pick,
            precision=lax.Precision.HIGHEST,
            preferred_element_type=jnp.float32,
        )
        total = part if total is None else total + part
    return total


def on_device(fields, shifts):
    row_count = fields.shape[1]
    rad_index = lax.axis_index("rad")
    total_rows = row_count * lax.axis_size("rad")
    inner_rows = (rad_index * row_count + jnp.arange(row_count, dtype=jnp.int32)).astype(
        jnp.float32
    )
    courant_inner = courant_profile(inner_rows, total_rows)
    initial = to_conserved(fields)
    section_one = initial + change(fields, courant_inner)
    section_one_prim = to_primitive(section_one)
    section_two = 0.5 * initial + 0.5 * (section_one + change(section_one_prim, courant_inner))
    return shift_rows(to_primitive(section_two), shifts)


def solution(mesh):
    in_specs = (P(None, "rad", None, "az"), P("rad"))
    out_specs = P(None, "rad", None, "az")
    return jax.shard_map(
        on_device, mesh=mesh, in_specs=in_specs, out_specs=out_specs, check_vma=False
    )
```

```python
import jax
import jax.numpy as jnp
from jax import lax
from jax.sharding import PartitionSpec as P


ADIABATIC = 1.4
COURANT_RADIAL = 0.09
COURANT_POLAR = 0.08
COURANT_AZIMUTH = 0.18


def shifted(block, axis, distance):
    devices = range(lax.axis_size(axis))
    route = [((i - distance) % len(devices), i) for i in devices]
    return lax.ppermute(block, axis, route)


def cut_along(values, first_cell, finish, along):
    return lax.slice_in_dim(values, first_cell, finish, axis=along)


def edge_states(values, along):
    length = values.shape[along]
    before = cut_along(values, 0, length - 3, along)
    centre = cut_along(values, 1, length - 2, along)
    follow = cut_along(values, 2, length - 1, along)
    beyond = cut_along(values, 3, length, along)
    interface = 7.0 / 12.0 * (centre + follow) - 1.0 / 12.0 * (before + beyond)
    interface = jnp.clip(interface, jnp.minimum(centre, follow), jnp.maximum(centre, follow))
    count = length - 3
    left_edge = cut_along(interface, 0, count - 1, along)
    right_edge = cut_along(interface, 1, count, along)
    middle_cell = cut_along(values, 2, length - 2, along)
    no_slope = (right_edge - middle_cell) * (middle_cell - left_edge) <= 0.0
    left_edge = jnp.where(no_slope, middle_cell, left_edge)
    right_edge = jnp.where(no_slope, middle_cell, right_edge)
    spread = right_edge - left_edge
    middle = middle_cell - 0.5 * (left_edge + right_edge)
    new_left = jnp.where(
        spread * middle > spread * spread / 6.0, 3.0 * middle_cell - 2.0 * right_edge, left_edge
    )
    new_right = jnp.where(
        spread * middle < -spread * spread / 6.0, 3.0 * middle_cell - 2.0 * left_edge, right_edge
    )
    return (new_left, new_right)


def primitive_parts(state, normal):
    density = state[0]
    pressure = state[4]
    normal_speed = state[normal]
    squared = state[1] * state[1] + state[2] * state[2] + state[3] * state[3]
    energy = pressure / (ADIABATIC - 1.0) + 0.5 * density * squared
    sound_speed = jnp.sqrt(ADIABATIC * pressure / density)
    conserved = [density, density * state[1], density * state[2], density * state[3], energy]
    flux_list = [plain_term * normal_speed for plain_term in conserved]
    flux_list[normal] = flux_list[normal] + pressure
    flux_list[4] = flux_list[4] + pressure * normal_speed
    return (density, pressure, normal_speed, energy, sound_speed, conserved, flux_list)


def star_flux(state, parts, wave_speed, contact, normal):
    density, pressure, normal_speed, energy, _, conserved, flux_list = parts
    factor = density * (wave_speed - normal_speed) / (wave_speed - contact)
    star_energy = factor * (
        energy / density
        + (contact - normal_speed) * (contact + pressure / (density * (wave_speed - normal_speed)))
    )
    star_state = [factor, factor * state[1], factor * state[2], factor * state[3], star_energy]
    star_state[normal] = factor * contact
    return [
        flux_term + wave_speed * (star_term - plain_term)
        for flux_term, star_term, plain_term in zip(flux_list, star_state, conserved)
    ]


def riemann_flux(left_state, right_state, normal):
    left_parts = primitive_parts(left_state, normal)
    right_parts = primitive_parts(right_state, normal)
    slow_wave = jnp.minimum(left_parts[2] - left_parts[4], right_parts[2] - right_parts[4])
    fast_wave = jnp.maximum(left_parts[2] + left_parts[4], right_parts[2] + right_parts[4])
    mass_left = left_parts[0] * (left_parts[2] - slow_wave)
    mass_right = right_parts[0] * (fast_wave - right_parts[2])
    contact = (
        mass_left * left_parts[2] + mass_right * right_parts[2] + left_parts[1] - right_parts[1]
    ) / (mass_left + mass_right)
    star_left = star_flux(left_state, left_parts, slow_wave, contact, normal)
    star_right = star_flux(right_state, right_parts, fast_wave, contact, normal)
    merged = []
    for flux_left, inner_left, inner_right, flux_right in zip(
        left_parts[6], star_left, star_right, right_parts[6]
    ):
        merged.append(
            jnp.where(
                slow_wave >= 0.0,
                flux_left,
                jnp.where(
                    contact >= 0.0, inner_left, jnp.where(fast_wave > 0.0, inner_right, flux_right)
                ),
            )
        )
    return jnp.stack(merged)


def flux_difference(window, along, normal):
    left_edge, right_edge = edge_states(window, along)
    cell_total = left_edge.shape[along]
    from_left = cut_along(right_edge, 0, cell_total - 1, along)
    from_right = cut_along(left_edge, 1, cell_total, along)
    flux_all = riemann_flux(from_left, from_right, normal)
    faces = flux_all.shape[along]
    return cut_along(flux_all, 1, faces, along) - cut_along(flux_all, 0, faces - 1, along)


def tendency(along_rad, along_az, inner, courant_rows):
    radial_term = flux_difference(along_rad, 1, 1)
    polar_term = flux_difference(
        jnp.pad(inner, ((0, 0), (0, 0), (3, 3), (0, 0)), mode="edge"), 2, 2
    )
    azimuth_term = flux_difference(along_az, 3, 3)
    return -(
        COURANT_RADIAL * radial_term
        + COURANT_POLAR * polar_term
        + courant_rows[None, :, None, None] * azimuth_term
    )


def courant_profile(row_index, total_rows):
    return COURANT_AZIMUTH / (1.0 + (row_index + 0.5) / total_rows)


def to_conserved(primitive):
    density = primitive[0]
    squared = (
        primitive[1] * primitive[1] + primitive[2] * primitive[2] + primitive[3] * primitive[3]
    )
    energy = primitive[4] / (ADIABATIC - 1.0) + 0.5 * density * squared
    return jnp.stack(
        [density, density * primitive[1], density * primitive[2], density * primitive[3], energy]
    )


def to_primitive(conserved):
    density = conserved[0]
    velocity = conserved[1:4] / density
    squared = velocity[0] * velocity[0] + velocity[1] * velocity[1] + velocity[2] * velocity[2]
    pressure = (ADIABATIC - 1.0) * (conserved[4] - 0.5 * density * squared)
    return jnp.concatenate([density[None], velocity, pressure[None]])


MAX_SHIFT = 768
HALO = 3


def ring_pairs(count, step, wrap):
    if wrap:
        return [(i, (i + step) % count) for i in range(count)]
    return [(i, i + step) for i in range(count) if 0 <= i + step < count]


def clamp_rows(block, depth):
    rad_index = lax.axis_index("rad")
    last_index = lax.axis_size("rad") - 1
    rows = block.shape[1]
    lower = jnp.where(
        rad_index == 0,
        jnp.broadcast_to(block[:, depth : depth + 1], block[:, :depth].shape),
        block[:, :depth],
    )
    upper = jnp.where(
        rad_index == last_index,
        jnp.broadcast_to(block[:, rows - depth - 1 : rows - depth], block[:, rows - depth :].shape),
        block[:, rows - depth :],
    )
    return jnp.concatenate([lower, block[:, depth : rows - depth], upper], axis=1)


def halos(x, width):
    n_rad, n_az = lax.axis_size("rad"), lax.axis_size("az")
    from_below = lax.ppermute(x[:, -width:], "rad", ring_pairs(n_rad, 1, False))
    from_above = lax.ppermute(x[:, :width], "rad", ring_pairs(n_rad, -1, False))
    from_left = lax.ppermute(x[..., -width:], "az", ring_pairs(n_az, 1, True))
    from_right = lax.ppermute(x[..., :width], "az", ring_pairs(n_az, -1, True))
    along_rad = clamp_rows(jnp.concatenate([from_below, x, from_above], axis=1), width)
    along_az = jnp.concatenate([from_left, x, from_right], axis=3)
    return along_rad, along_az


def change(x, courant_rows):
    along_rad, along_az = halos(x, HALO)
    return tendency(along_rad, along_az, x, courant_rows)


def shift_rows(primitive, shifts):
    cell_count = primitive.shape[3]
    far = -(-MAX_SHIFT // cell_count)
    blocks = [primitive]
    for distance in range(1, far + 1):
        if distance <= 2:
            blocks.append(shifted(primitive, "az", distance))
        else:
            blocks.append(shifted(blocks[-1], "az", 1))
    source = lax.broadcasted_iota(jnp.int32, (1, cell_count, cell_count), 1)
    target = lax.broadcasted_iota(jnp.int32, (1, cell_count, cell_count), 2)
    offset = source - target + shifts[:, None, None]
    total = None
    for distance, block in enumerate(blocks):
        pick = (offset == distance * cell_count).astype(jnp.float32)
        part = jnp.einsum(
            "fitk,ikc->fitc",
            block,
            pick,
            precision=lax.Precision.HIGHEST,
            preferred_element_type=jnp.float32,
        )
        total = part if total is None else total + part
    return total


def on_device(fields, shifts):
    row_count = fields.shape[1]
    rad_index = lax.axis_index("rad")
    total_rows = row_count * lax.axis_size("rad")
    inner_rows = (rad_index * row_count + jnp.arange(row_count, dtype=jnp.int32)).astype(
        jnp.float32
    )
    courant_inner = courant_profile(inner_rows, total_rows)
    initial = to_conserved(fields)
    section_one = initial + change(fields, courant_inner)
    section_one_prim = to_primitive(section_one)
    section_two = 0.5 * initial + 0.5 * (
        section_one + change(section_one_prim, courant_inner)
    )
    return shift_rows(to_primitive(section_two), shifts)


def solution(mesh):
    in_specs = (P(None, "rad", None, "az"), P("rad"))
    out_specs = P(None, "rad", None, "az")
    return jax.shard_map(
        on_device, mesh=mesh, in_specs=in_specs, out_specs=out_specs, check_vma=False
    )
```

```python
import jax
import jax.numpy as jnp
from jax import lax
from jax.sharding import PartitionSpec as P


ADIABATIC = 1.4
COURANT_RADIAL = 0.09
COURANT_POLAR = 0.08
COURANT_AZIMUTH = 0.18


def shifted(block, axis, distance):
    devices = range(lax.axis_size(axis))
    route = [((i - distance) % len(devices), i) for i in devices]
    return lax.ppermute(block, axis, route)


def cut_along(values, first_cell, finish, along):
    return lax.slice_in_dim(values, first_cell, finish, axis=along)


def edge_states(values, along):
    length = values.shape[along]
    before = cut_along(values, 0, length - 3, along)
    centre = cut_along(values, 1, length - 2, along)
    follow = cut_along(values, 2, length - 1, along)
    beyond = cut_along(values, 3, length, along)
    interface = 7.0 / 12.0 * (centre + follow) - 1.0 / 12.0 * (before + beyond)
    interface = jnp.clip(interface, jnp.minimum(centre, follow), jnp.maximum(centre, follow))
    count = length - 3
    left_edge = cut_along(interface, 0, count - 1, along)
    right_edge = cut_along(interface, 1, count, along)
    middle_cell = cut_along(values, 2, length - 2, along)
    no_slope = (right_edge - middle_cell) * (middle_cell - left_edge) <= 0.0
    left_edge = jnp.where(no_slope, middle_cell, left_edge)
    right_edge = jnp.where(no_slope, middle_cell, right_edge)
    spread = right_edge - left_edge
    middle = middle_cell - 0.5 * (left_edge + right_edge)
    new_left = jnp.where(
        spread * middle > spread * spread / 6.0, 3.0 * middle_cell - 2.0 * right_edge, left_edge
    )
    new_right = jnp.where(
        spread * middle < -spread * spread / 6.0, 3.0 * middle_cell - 2.0 * left_edge, right_edge
    )
    return (new_left, new_right)


def primitive_parts(state, normal):
    density = state[0]
    pressure = state[4]
    normal_speed = state[normal]
    squared = state[1] * state[1] + state[2] * state[2] + state[3] * state[3]
    energy = pressure / (ADIABATIC - 1.0) + 0.5 * density * squared
    sound_speed = jnp.sqrt(ADIABATIC * pressure / density)
    conserved = [density, density * state[1], density * state[2], density * state[3], energy]
    flux_list = [plain_term * normal_speed for plain_term in conserved]
    flux_list[normal] = flux_list[normal] + pressure
    flux_list[4] = flux_list[4] + pressure * normal_speed
    return (density, pressure, normal_speed, energy, sound_speed, conserved, flux_list)


def star_flux(state, parts, wave_speed, contact, normal):
    density, pressure, normal_speed, energy, _, conserved, flux_list = parts
    factor = density * (wave_speed - normal_speed) / (wave_speed - contact)
    star_energy = factor * (
        energy / density
        + (contact - normal_speed) * (contact + pressure / (density * (wave_speed - normal_speed)))
    )
    star_state = [factor, factor * state[1], factor * state[2], factor * state[3], star_energy]
    star_state[normal] = factor * contact
    return [
        flux_term + wave_speed * (star_term - plain_term)
        for flux_term, star_term, plain_term in zip(flux_list, star_state, conserved)
    ]


def riemann_flux(left_state, right_state, normal):
    left_parts = primitive_parts(left_state, normal)
    right_parts = primitive_parts(right_state, normal)
    slow_wave = jnp.minimum(left_parts[2] - left_parts[4], right_parts[2] - right_parts[4])
    fast_wave = jnp.maximum(left_parts[2] + left_parts[4], right_parts[2] + right_parts[4])
    mass_left = left_parts[0] * (left_parts[2] - slow_wave)
    mass_right = right_parts[0] * (fast_wave - right_parts[2])
    contact = (
        mass_left * left_parts[2] + mass_right * right_parts[2] + left_parts[1] - right_parts[1]
    ) / (mass_left + mass_right)
    star_left = star_flux(left_state, left_parts, slow_wave, contact, normal)
    star_right = star_flux(right_state, right_parts, fast_wave, contact, normal)
    merged = []
    for flux_left, inner_left, inner_right, flux_right in zip(
        left_parts[6], star_left, star_right, right_parts[6]
    ):
        merged.append(
            jnp.where(
                slow_wave >= 0.0,
                flux_left,
                jnp.where(
                    contact >= 0.0, inner_left, jnp.where(fast_wave > 0.0, inner_right, flux_right)
                ),
            )
        )
    return jnp.stack(merged)


def flux_difference(window, along, normal):
    left_edge, right_edge = edge_states(window, along)
    cell_total = left_edge.shape[along]
    from_left = cut_along(right_edge, 0, cell_total - 1, along)
    from_right = cut_along(left_edge, 1, cell_total, along)
    flux_all = riemann_flux(from_left, from_right, normal)
    faces = flux_all.shape[along]
    return cut_along(flux_all, 1, faces, along) - cut_along(flux_all, 0, faces - 1, along)


def tendency(along_rad, along_az, inner, courant_rows):
    radial_term = flux_difference(along_rad, 1, 1)
    polar_term = flux_difference(
        jnp.pad(inner, ((0, 0), (0, 0), (3, 3), (0, 0)), mode="edge"), 2, 2
    )
    azimuth_term = flux_difference(along_az, 3, 3)
    return -(
        COURANT_RADIAL * radial_term
        + COURANT_POLAR * polar_term
        + courant_rows[None, :, None, None] * azimuth_term
    )


def courant_profile(row_index, total_rows):
    return COURANT_AZIMUTH / (1.0 + (row_index + 0.5) / total_rows)


def to_conserved(primitive):
    density = primitive[0]
    squared = (
        primitive[1] * primitive[1] + primitive[2] * primitive[2] + primitive[3] * primitive[3]
    )
    energy = primitive[4] / (ADIABATIC - 1.0) + 0.5 * density * squared
    return jnp.stack(
        [density, density * primitive[1], density * primitive[2], density * primitive[3], energy]
    )


def to_primitive(conserved):
    density = conserved[0]
    velocity = conserved[1:4] / density
    squared = velocity[0] * velocity[0] + velocity[1] * velocity[1] + velocity[2] * velocity[2]
    pressure = (ADIABATIC - 1.0) * (conserved[4] - 0.5 * density * squared)
    return jnp.concatenate([density[None], velocity, pressure[None]])


MAX_SHIFT = 768
HALO = 3


def ring_pairs(count, step, wrap):
    if wrap:
        return [(i, (i + step) % count) for i in range(count)]
    return [(i, i + step) for i in range(count) if 0 <= i + step < count]


def clamp_rows(block, depth):
    rad_index = lax.axis_index("rad")
    last_index = lax.axis_size("rad") - 1
    rows = block.shape[1]
    lower = jnp.where(
        rad_index == 0,
        jnp.broadcast_to(block[:, depth : depth + 1], block[:, :depth].shape),
        block[:, :depth],
    )
    upper = jnp.where(
        rad_index == last_index,
        jnp.broadcast_to(block[:, rows - depth - 1 : rows - depth], block[:, rows - depth :].shape),
        block[:, rows - depth :],
    )
    return jnp.concatenate([lower, block[:, depth : rows - depth], upper], axis=1)


def halos(x, width):
    n_rad, n_az = lax.axis_size("rad"), lax.axis_size("az")
    from_below = lax.ppermute(x[:, -width:], "rad", ring_pairs(n_rad, 1, False))
    from_above = lax.ppermute(x[:, :width], "rad", ring_pairs(n_rad, -1, False))
    from_left = lax.ppermute(x[..., -width:], "az", ring_pairs(n_az, 1, True))
    from_right = lax.ppermute(x[..., :width], "az", ring_pairs(n_az, -1, True))
    along_rad = clamp_rows(jnp.concatenate([from_below, x, from_above], axis=1), width)
    along_az = jnp.concatenate([from_left, x, from_right], axis=3)
    return along_rad, along_az


def change(x, courant_rows):
    along_rad, along_az = halos(x, HALO)
    return tendency(along_rad, along_az, x, courant_rows)


def shift_rows(primitive, shifts):
    cell_count = primitive.shape[3]
    far = -(-MAX_SHIFT // cell_count)
    blocks = [primitive]
    for distance in range(1, far + 1):
        if distance <= 2:
            blocks.append(shifted(primitive, "az", distance))
        else:
            blocks.append(shifted(blocks[-1], "az", 1))
    source = lax.broadcasted_iota(jnp.int32, (1, cell_count, cell_count), 1)
    target = lax.broadcasted_iota(jnp.int32, (1, cell_count, cell_count), 2)
    offset = source - target + shifts[:, None, None]
    total = None
    arrival = [0] + list(range(2, far + 1))[:1] + [1] + list(range(3, far + 1))
    arrival = [d for d in arrival if d < len(blocks)]
    for distance in arrival:
        block = blocks[distance]
        pick = (offset == distance * cell_count).astype(jnp.float32)
        part = jnp.einsum(
            "fitk,ikc->fitc",
            block,
            pick,
            precision=lax.Precision.HIGHEST,
            preferred_element_type=jnp.float32,
        )
        total = part if total is None else total + part
    return total


def on_device(fields, shifts):
    row_count = fields.shape[1]
    rad_index = lax.axis_index("rad")
    total_rows = row_count * lax.axis_size("rad")
    inner_rows = (rad_index * row_count + jnp.arange(row_count, dtype=jnp.int32)).astype(
        jnp.float32
    )
    courant_inner = courant_profile(inner_rows, total_rows)
    initial = to_conserved(fields)
    section_one = initial + change(fields, courant_inner)
    section_one_prim = to_primitive(section_one)
    section_two = 0.5 * initial + 0.5 * (
        section_one + change(section_one_prim, courant_inner)
    )
    return shift_rows(to_primitive(section_two), shifts)


def solution(mesh):
    in_specs = (P(None, "rad", None, "az"), P("rad"))
    out_specs = P(None, "rad", None, "az")
    return jax.shard_map(
        on_device, mesh=mesh, in_specs=in_specs, out_specs=out_specs, check_vma=False
    )
```

```python
import jax
import jax.numpy as jnp
from jax import lax
from jax.sharding import PartitionSpec as P


ADIABATIC = 1.4
COURANT_RADIAL = 0.09
COURANT_POLAR = 0.08
COURANT_AZIMUTH = 0.18


def shifted(block, axis, distance):
    devices = range(lax.axis_size(axis))
    route = [((i - distance) % len(devices), i) for i in devices]
    return lax.ppermute(block, axis, route)


def cut_along(values, first_cell, finish, along):
    return lax.slice_in_dim(values, first_cell, finish, axis=along)


def edge_states(values, along):
    length = values.shape[along]
    before = cut_along(values, 0, length - 3, along)
    centre = cut_along(values, 1, length - 2, along)
    follow = cut_along(values, 2, length - 1, along)
    beyond = cut_along(values, 3, length, along)
    interface = 7.0 / 12.0 * (centre + follow) - 1.0 / 12.0 * (before + beyond)
    interface = jnp.clip(interface, jnp.minimum(centre, follow), jnp.maximum(centre, follow))
    count = length - 3
    left_edge = cut_along(interface, 0, count - 1, along)
    right_edge = cut_along(interface, 1, count, along)
    middle_cell = cut_along(values, 2, length - 2, along)
    no_slope = (right_edge - middle_cell) * (middle_cell - left_edge) <= 0.0
    left_edge = jnp.where(no_slope, middle_cell, left_edge)
    right_edge = jnp.where(no_slope, middle_cell, right_edge)
    spread = right_edge - left_edge
    middle = middle_cell - 0.5 * (left_edge + right_edge)
    new_left = jnp.where(
        spread * middle > spread * spread / 6.0, 3.0 * middle_cell - 2.0 * right_edge, left_edge
    )
    new_right = jnp.where(
        spread * middle < -spread * spread / 6.0, 3.0 * middle_cell - 2.0 * left_edge, right_edge
    )
    return (new_left, new_right)


def primitive_parts(state, normal):
    density = state[0]
    pressure = state[4]
    normal_speed = state[normal]
    squared = state[1] * state[1] + state[2] * state[2] + state[3] * state[3]
    energy = pressure / (ADIABATIC - 1.0) + 0.5 * density * squared
    sound_speed = jnp.sqrt(ADIABATIC * pressure / density)
    conserved = [density, density * state[1], density * state[2], density * state[3], energy]
    flux_list = [plain_term * normal_speed for plain_term in conserved]
    flux_list[normal] = flux_list[normal] + pressure
    flux_list[4] = flux_list[4] + pressure * normal_speed
    return (density, pressure, normal_speed, energy, sound_speed, conserved, flux_list)


def star_flux(state, parts, wave_speed, contact, normal):
    density, pressure, normal_speed, energy, _, conserved, flux_list = parts
    factor = density * (wave_speed - normal_speed) / (wave_speed - contact)
    star_energy = factor * (
        energy / density
        + (contact - normal_speed) * (contact + pressure / (density * (wave_speed - normal_speed)))
    )
    star_state = [factor, factor * state[1], factor * state[2], factor * state[3], star_energy]
    star_state[normal] = factor * contact
    return [
        flux_term + wave_speed * (star_term - plain_term)
        for flux_term, star_term, plain_term in zip(flux_list, star_state, conserved)
    ]


def riemann_flux(left_state, right_state, normal):
    left_parts = primitive_parts(left_state, normal)
    right_parts = primitive_parts(right_state, normal)
    slow_wave = jnp.minimum(left_parts[2] - left_parts[4], right_parts[2] - right_parts[4])
    fast_wave = jnp.maximum(left_parts[2] + left_parts[4], right_parts[2] + right_parts[4])
    mass_left = left_parts[0] * (left_parts[2] - slow_wave)
    mass_right = right_parts[0] * (fast_wave - right_parts[2])
    contact = (
        mass_left * left_parts[2] + mass_right * right_parts[2] + left_parts[1] - right_parts[1]
    ) / (mass_left + mass_right)
    star_left = star_flux(left_state, left_parts, slow_wave, contact, normal)
    star_right = star_flux(right_state, right_parts, fast_wave, contact, normal)
    merged = []
    for flux_left, inner_left, inner_right, flux_right in zip(
        left_parts[6], star_left, star_right, right_parts[6]
    ):
        merged.append(
            jnp.where(
                slow_wave >= 0.0,
                flux_left,
                jnp.where(
                    contact >= 0.0, inner_left, jnp.where(fast_wave > 0.0, inner_right, flux_right)
                ),
            )
        )
    return jnp.stack(merged)


def flux_difference(window, along, normal):
    left_edge, right_edge = edge_states(window, along)
    cell_total = left_edge.shape[along]
    from_left = cut_along(right_edge, 0, cell_total - 1, along)
    from_right = cut_along(left_edge, 1, cell_total, along)
    flux_all = riemann_flux(from_left, from_right, normal)
    faces = flux_all.shape[along]
    return cut_along(flux_all, 1, faces, along) - cut_along(flux_all, 0, faces - 1, along)


def tendency(along_rad, along_az, inner, courant_rows):
    radial_term = flux_difference(along_rad, 1, 1)
    polar_term = flux_difference(
        jnp.pad(inner, ((0, 0), (0, 0), (3, 3), (0, 0)), mode="edge"), 2, 2
    )
    azimuth_term = flux_difference(along_az, 3, 3)
    return -(
        COURANT_RADIAL * radial_term
        + COURANT_POLAR * polar_term
        + courant_rows[None, :, None, None] * azimuth_term
    )


def courant_profile(row_index, total_rows):
    return COURANT_AZIMUTH / (1.0 + (row_index + 0.5) / total_rows)


def to_conserved(primitive):
    density = primitive[0]
    squared = (
        primitive[1] * primitive[1] + primitive[2] * primitive[2] + primitive[3] * primitive[3]
    )
    energy = primitive[4] / (ADIABATIC - 1.0) + 0.5 * density * squared
    return jnp.stack(
        [density, density * primitive[1], density * primitive[2], density * primitive[3], energy]
    )


def to_primitive(conserved):
    density = conserved[0]
    velocity = conserved[1:4] / density
    squared = velocity[0] * velocity[0] + velocity[1] * velocity[1] + velocity[2] * velocity[2]
    pressure = (ADIABATIC - 1.0) * (conserved[4] - 0.5 * density * squared)
    return jnp.concatenate([density[None], velocity, pressure[None]])


MAX_SHIFT = 768
HALO = 3


def ring_pairs(count, step, wrap):
    if wrap:
        return [(i, (i + step) % count) for i in range(count)]
    return [(i, i + step) for i in range(count) if 0 <= i + step < count]


def clamp_rows(block, depth):
    rad_index = lax.axis_index("rad")
    last_index = lax.axis_size("rad") - 1
    rows = block.shape[1]
    lower = jnp.where(
        rad_index == 0,
        jnp.broadcast_to(block[:, depth : depth + 1], block[:, :depth].shape),
        block[:, :depth],
    )
    upper = jnp.where(
        rad_index == last_index,
        jnp.broadcast_to(block[:, rows - depth - 1 : rows - depth], block[:, rows - depth :].shape),
        block[:, rows - depth :],
    )
    return jnp.concatenate([lower, block[:, depth : rows - depth], upper], axis=1)


def halos(x, width):
    n_rad, n_az = lax.axis_size("rad"), lax.axis_size("az")
    from_below = lax.ppermute(x[:, -width:], "rad", ring_pairs(n_rad, 1, False))
    from_above = lax.ppermute(x[:, :width], "rad", ring_pairs(n_rad, -1, False))
    from_left = lax.ppermute(x[..., -width:], "az", ring_pairs(n_az, 1, True))
    from_right = lax.ppermute(x[..., :width], "az", ring_pairs(n_az, -1, True))
    along_rad = clamp_rows(jnp.concatenate([from_below, x, from_above], axis=1), width)
    along_az = jnp.concatenate([from_left, x, from_right], axis=3)
    return along_rad, along_az


def change(x, courant_rows):
    along_rad, along_az = halos(x, HALO)
    return tendency(along_rad, along_az, x, courant_rows)


def shift_rows(primitive, shifts):
    cell_count = primitive.shape[3]
    far = -(-MAX_SHIFT // cell_count)
    blocks = [primitive]
    for _ in range(1, far + 1):
        blocks.append(shifted(blocks[-1], "az", 1))
    source = lax.broadcasted_iota(jnp.int32, (1, cell_count, cell_count), 1)
    target = lax.broadcasted_iota(jnp.int32, (1, cell_count, cell_count), 2)
    offset = source - target + shifts[:, None, None]
    total = None
    for distance in range(len(blocks)):
        block = blocks[distance]
        pick = (offset == distance * cell_count).astype(jnp.float32)
        part = jnp.einsum(
            "fitk,ikc->fitc",
            block,
            pick,
            precision=lax.Precision.HIGHEST,
            preferred_element_type=jnp.float32,
        )
        total = part if total is None else total + part
    return total


def on_device(fields, shifts):
    row_count = fields.shape[1]
    rad_index = lax.axis_index("rad")
    total_rows = row_count * lax.axis_size("rad")
    inner_rows = (rad_index * row_count + jnp.arange(row_count, dtype=jnp.int32)).astype(
        jnp.float32
    )
    courant_inner = courant_profile(inner_rows, total_rows)
    initial = to_conserved(fields)
    section_one = initial + change(fields, courant_inner)
    section_one_prim = to_primitive(section_one)
    section_two = 0.5 * initial + 0.5 * (
        section_one + change(section_one_prim, courant_inner)
    )
    return shift_rows(to_primitive(section_two), shifts)


def solution(mesh):
    in_specs = (P(None, "rad", None, "az"), P("rad"))
    out_specs = P(None, "rad", None, "az")
    return jax.shard_map(
        on_device, mesh=mesh, in_specs=in_specs, out_specs=out_specs, check_vma=False
    )
```

```python
import jax
import jax.numpy as jnp
from jax import lax
from jax.sharding import PartitionSpec as P


ADIABATIC = 1.4
COURANT_RADIAL = 0.09
COURANT_POLAR = 0.08
COURANT_AZIMUTH = 0.18


def shifted(block, axis, distance):
    devices = range(lax.axis_size(axis))
    route = [((i - distance) % len(devices), i) for i in devices]
    return lax.ppermute(block, axis, route)


def cut_along(values, first_cell, finish, along):
    return lax.slice_in_dim(values, first_cell, finish, axis=along)


def edge_states(values, along):
    length = values.shape[along]
    before = cut_along(values, 0, length - 3, along)
    centre = cut_along(values, 1, length - 2, along)
    follow = cut_along(values, 2, length - 1, along)
    beyond = cut_along(values, 3, length, along)
    interface = 7.0 / 12.0 * (centre + follow) - 1.0 / 12.0 * (before + beyond)
    interface = jnp.clip(interface, jnp.minimum(centre, follow), jnp.maximum(centre, follow))
    count = length - 3
    left_edge = cut_along(interface, 0, count - 1, along)
    right_edge = cut_along(interface, 1, count, along)
    middle_cell = cut_along(values, 2, length - 2, along)
    no_slope = (right_edge - middle_cell) * (middle_cell - left_edge) <= 0.0
    left_edge = jnp.where(no_slope, middle_cell, left_edge)
    right_edge = jnp.where(no_slope, middle_cell, right_edge)
    spread = right_edge - left_edge
    middle = middle_cell - 0.5 * (left_edge + right_edge)
    new_left = jnp.where(
        spread * middle > spread * spread / 6.0, 3.0 * middle_cell - 2.0 * right_edge, left_edge
    )
    new_right = jnp.where(
        spread * middle < -spread * spread / 6.0, 3.0 * middle_cell - 2.0 * left_edge, right_edge
    )
    return (new_left, new_right)


def primitive_parts(state, normal):
    density = state[0]
    pressure = state[4]
    normal_speed = state[normal]
    squared = state[1] * state[1] + state[2] * state[2] + state[3] * state[3]
    energy = pressure / (ADIABATIC - 1.0) + 0.5 * density * squared
    sound_speed = jnp.sqrt(ADIABATIC * pressure / density)
    conserved = [density, density * state[1], density * state[2], density * state[3], energy]
    flux_list = [plain_term * normal_speed for plain_term in conserved]
    flux_list[normal] = flux_list[normal] + pressure
    flux_list[4] = flux_list[4] + pressure * normal_speed
    return (density, pressure, normal_speed, energy, sound_speed, conserved, flux_list)


def star_flux(state, parts, wave_speed, contact, normal):
    density, pressure, normal_speed, energy, _, conserved, flux_list = parts
    factor = density * (wave_speed - normal_speed) / (wave_speed - contact)
    star_energy = factor * (
        energy / density
        + (contact - normal_speed) * (contact + pressure / (density * (wave_speed - normal_speed)))
    )
    star_state = [factor, factor * state[1], factor * state[2], factor * state[3], star_energy]
    star_state[normal] = factor * contact
    return [
        flux_term + wave_speed * (star_term - plain_term)
        for flux_term, star_term, plain_term in zip(flux_list, star_state, conserved)
    ]


def riemann_flux(left_state, right_state, normal):
    left_parts = primitive_parts(left_state, normal)
    right_parts = primitive_parts(right_state, normal)
    slow_wave = jnp.minimum(left_parts[2] - left_parts[4], right_parts[2] - right_parts[4])
    fast_wave = jnp.maximum(left_parts[2] + left_parts[4], right_parts[2] + right_parts[4])
    mass_left = left_parts[0] * (left_parts[2] - slow_wave)
    mass_right = right_parts[0] * (fast_wave - right_parts[2])
    contact = (
        mass_left * left_parts[2] + mass_right * right_parts[2] + left_parts[1] - right_parts[1]
    ) / (mass_left + mass_right)
    star_left = star_flux(left_state, left_parts, slow_wave, contact, normal)
    star_right = star_flux(right_state, right_parts, fast_wave, contact, normal)
    merged = []
    for flux_left, inner_left, inner_right, flux_right in zip(
        left_parts[6], star_left, star_right, right_parts[6]
    ):
        merged.append(
            jnp.where(
                slow_wave >= 0.0,
                flux_left,
                jnp.where(
                    contact >= 0.0, inner_left, jnp.where(fast_wave > 0.0, inner_right, flux_right)
                ),
            )
        )
    return jnp.stack(merged)


def flux_difference(window, along, normal):
    left_edge, right_edge = edge_states(window, along)
    cell_total = left_edge.shape[along]
    from_left = cut_along(right_edge, 0, cell_total - 1, along)
    from_right = cut_along(left_edge, 1, cell_total, along)
    flux_all = riemann_flux(from_left, from_right, normal)
    faces = flux_all.shape[along]
    return cut_along(flux_all, 1, faces, along) - cut_along(flux_all, 0, faces - 1, along)


def tendency(along_rad, along_az, inner, courant_rows):
    radial_term = flux_difference(along_rad, 1, 1)
    polar_term = flux_difference(
        jnp.pad(inner, ((0, 0), (0, 0), (3, 3), (0, 0)), mode="edge"), 2, 2
    )
    azimuth_term = flux_difference(along_az, 3, 3)
    return -(
        COURANT_RADIAL * radial_term
        + COURANT_POLAR * polar_term
        + courant_rows[None, :, None, None] * azimuth_term
    )


def courant_profile(row_index, total_rows):
    return COURANT_AZIMUTH / (1.0 + (row_index + 0.5) / total_rows)


def to_conserved(primitive):
    density = primitive[0]
    squared = (
        primitive[1] * primitive[1] + primitive[2] * primitive[2] + primitive[3] * primitive[3]
    )
    energy = primitive[4] / (ADIABATIC - 1.0) + 0.5 * density * squared
    return jnp.stack(
        [density, density * primitive[1], density * primitive[2], density * primitive[3], energy]
    )


def to_primitive(conserved):
    density = conserved[0]
    velocity = conserved[1:4] / density
    squared = velocity[0] * velocity[0] + velocity[1] * velocity[1] + velocity[2] * velocity[2]
    pressure = (ADIABATIC - 1.0) * (conserved[4] - 0.5 * density * squared)
    return jnp.concatenate([density[None], velocity, pressure[None]])


MAX_SHIFT = 768
HALO = 3


def ring_pairs(count, step, wrap):
    if wrap:
        return [(i, (i + step) % count) for i in range(count)]
    return [(i, i + step) for i in range(count) if 0 <= i + step < count]


def clamp_rows(block, depth):
    rad_index = lax.axis_index("rad")
    last_index = lax.axis_size("rad") - 1
    rows = block.shape[1]
    lower = jnp.where(
        rad_index == 0,
        jnp.broadcast_to(block[:, depth : depth + 1], block[:, :depth].shape),
        block[:, :depth],
    )
    upper = jnp.where(
        rad_index == last_index,
        jnp.broadcast_to(block[:, rows - depth - 1 : rows - depth], block[:, rows - depth :].shape),
        block[:, rows - depth :],
    )
    return jnp.concatenate([lower, block[:, depth : rows - depth], upper], axis=1)


def halos(x, width):
    n_rad, n_az = lax.axis_size("rad"), lax.axis_size("az")
    from_below = lax.ppermute(x[:, -width:], "rad", ring_pairs(n_rad, 1, False))
    from_above = lax.ppermute(x[:, :width], "rad", ring_pairs(n_rad, -1, False))
    from_left = lax.ppermute(x[..., -width:], "az", ring_pairs(n_az, 1, True))
    from_right = lax.ppermute(x[..., :width], "az", ring_pairs(n_az, -1, True))
    along_rad = clamp_rows(jnp.concatenate([from_below, x, from_above], axis=1), width)
    along_az = jnp.concatenate([from_left, x, from_right], axis=3)
    return along_rad, along_az


def change(x, courant_rows):
    along_rad, along_az = halos(x, HALO)
    return tendency(along_rad, along_az, x, courant_rows)


def shift_rows(primitive, shifts):
    cell_count = primitive.shape[3]
    far = -(-MAX_SHIFT // cell_count)
    blocks = [primitive]
    for distance in range(1, far + 1):
        blocks.append(shifted(primitive, "az", distance))
    source = lax.broadcasted_iota(jnp.int32, (1, cell_count, cell_count), 1)
    target = lax.broadcasted_iota(jnp.int32, (1, cell_count, cell_count), 2)
    offset = source - target + shifts[:, None, None]
    total = None
    arrival = [0, 1, 2, 3]
    arrival = [d for d in arrival if d < len(blocks)]
    for distance in arrival:
        block = blocks[distance]
        pick = (offset == distance * cell_count).astype(jnp.float32)
        part = jnp.einsum(
            "fitk,ikc->fitc",
            block,
            pick,
            precision=lax.Precision.HIGHEST,
            preferred_element_type=jnp.float32,
        )
        total = part if total is None else total + part
    return total


def on_device(fields, shifts):
    row_count = fields.shape[1]
    rad_index = lax.axis_index("rad")
    total_rows = row_count * lax.axis_size("rad")
    inner_rows = (rad_index * row_count + jnp.arange(row_count, dtype=jnp.int32)).astype(
        jnp.float32
    )
    courant_inner = courant_profile(inner_rows, total_rows)
    initial = to_conserved(fields)
    section_one = initial + change(fields, courant_inner)
    section_one_prim = to_primitive(section_one)
    section_two = 0.5 * initial + 0.5 * (
        section_one + change(section_one_prim, courant_inner)
    )
    return shift_rows(to_primitive(section_two), shifts)


def solution(mesh):
    in_specs = (P(None, "rad", None, "az"), P("rad"))
    out_specs = P(None, "rad", None, "az")
    return jax.shard_map(
        on_device, mesh=mesh, in_specs=in_specs, out_specs=out_specs, check_vma=False
    )
```
